512 devices in a mesh: rep: 16 (over y_lo, x, core), space: 32 (over y_hi, z).
Axes of the slice: x: 4, y: 8 (y_hi: 4, y_lo: 2; y = y_hi * 2 + y_lo), z: 8, core: 2. Of those that a mesh axis runs over, the one named last changes fastest.
Arguments:
- positions: float32 [16, 2048, 3, 128], P('rep', 'space'), may hold values from 0 to 0.6
- velocities: float32 [16, 2048, 3, 128], P('rep', 'space')
- strength: float32 [16, 2048, 128], P('rep', 'space'), may hold values from 0.5 to 1.5
- noise: float32 [4, 16, 2048, 128], P(None, 'rep', 'space'), may hold values from -4 to 4
- neighbours: int32 [16, 2048, 3], P('rep', 'space'), may hold values from 0 to 95, as said below
- bins: int32 [16, 2048, 128], P('rep', 'space'), may hold values from 0 to 1023, as said below
- thermal: float32 [16, 3, 128], P('rep'), may hold values from -3 to 3
- slot_counts: int32 [16], P('rep'), may hold values from 32 to 128, as said below
Outputs:
- new_positions: float32 [16, 2048, 3, 128], P('rep', 'space')
- new_velocities: float32 [16, 2048, 3, 128], P('rep', 'space')
- bin_velocity: float32 [3, 32768], P(None, 'space')
- inserted: float32 [16, 3, 128], P('rep')
The draws below stay inside these ranges and needn't reach their ends.
Inputs may be any that keep to these rules, and one draw needn't show every extreme that they name: `neighbours`: entry e names tile e - 16 counted from the first tile of the same slab. The first entry of every list is the tile itself, the second lies exactly 16 tiles away, the others are distinct, nonzero and at most 16 tiles away, and differ from the second. The beads of each replica in each slab name every one of the slab's 1024 bins at least once. `slot_counts`: some replica fills all 128 slots.
All inputs are finite; a program needn't handle non-finite values.
Results may differ from the reference program's by a relative error of at most 0.00014.
Values sent between devices are 32-bit elements; how exact they have to be, the bound alone decides.
No kernel may reach another device: no remote copies, remote signals or barrier semaphores. Data moves between devices by JAX's collectives and lax.ppermute only.
A program may use at most 64 MiB of HBM per device.

```python
import math
import jax
import jax.numpy as jnp
from jax import lax

TILE = 128
TILES_DEV = 64
HALO = 16
LINKS = 3
SUBSTEPS = 4
BINS_DEV = 1024
INSERT = 128
REPS = 16
TILES = 2048
BINS = 32768


def draw_velocities(key, part):
    first_key = jax.random.fold_in(key, 0)
    along = jnp.arange(TILES, dtype=jnp.float32) / max(TILES - 1, 1)
    across = jnp.arange(REPS, dtype=jnp.float32) / max(REPS - 1, 1)
    component = jnp.arange(3)[None, None, :, None]
    raw = 0.5 * jax.random.normal(first_key, (REPS, TILES, 3, TILE), jnp.float32)
    profile = 0.5 + along
    rep_scale = 0.5 + across
    mean_flow = rep_scale[:, None] * profile[None, :]
    return (raw + jnp.where(component == 0, mean_flow[:, :, None, None], 0.0)).astype(jnp.float32)


def tile_directions(key):
    side_key = jax.random.fold_in(key, 101)
    local = jnp.arange(TILES, dtype=jnp.int32) % TILES_DEV
    direction = 2 * jax.random.randint(side_key, (REPS, TILES), 0, 2) - 1
    direction = jnp.where(local[None, :] == 0, -1, direction)
    direction = jnp.where(local[None, :] == TILES_DEV - 1, 1, direction)
    return direction.astype(jnp.int32)


def draw_neighbours(key, part):
    score_key = jax.random.fold_in(key, 202)
    local = jnp.arange(TILES, dtype=jnp.int32) % TILES_DEV
    direction = tile_directions(key)
    candidates = jnp.concatenate([jnp.arange(-HALO, 0, dtype=jnp.int32), jnp.arange(1, HALO + 1, dtype=jnp.int32)])
    scores = jax.random.randint(score_key, (REPS, TILES, 2 * HALO), 0, 2 ** 20) * (2 * HALO) + jnp.arange(2 * HALO, dtype=jnp.int32)
    far_slot = jnp.where(direction > 0, 2 * HALO - 1, 0)
    scores = jnp.where(jnp.arange(2 * HALO)[None, None, :] == far_slot[:, :, None], 2 ** 30, scores)
    chosen = jnp.argsort(scores, axis=-1)[:, :, :LINKS - 2]
    others = candidates[chosen]
    offsets = jnp.concatenate([jnp.zeros((REPS, TILES, 1), jnp.int32), (direction * HALO)[:, :, None], others], axis=-1)
    return (offsets + local[None, :, None] + HALO).astype(jnp.int32)


def draw_noise(key, part):
    value_key = jax.random.fold_in(key, 303)
    direction = tile_directions(key).astype(jnp.float32)
    shape = (SUBSTEPS, REPS, TILES, TILE)
    rough = jnp.clip(jax.random.normal(value_key, shape, jnp.float32), -4.0, 4.0)
    tail = jnp.clip(rough, -1.5, 1.5) + 2.5 * direction[None, :, :, None]
    last = (jnp.arange(SUBSTEPS) == SUBSTEPS - 1)[:, None, None, None]
    return jnp.where(last, tail, rough).astype(jnp.float32)


def draw_bins(key, part):
    beads = TILES_DEV * TILE
    slabs = TILES // TILES_DEV

    def one_device(device_key):
        fill_key, perm_key = jax.random.split(device_key)
        slots = jnp.arange(beads, dtype=jnp.int32)
        spread = jax.random.randint(fill_key, (beads,), 0, BINS_DEV)
        labels = jnp.where(slots < BINS_DEV, slots, spread)
        return labels[jax.random.permutation(perm_key, beads)]
    labelled = jax.vmap(one_device)(jax.random.split(key, REPS * slabs))
    return labelled.reshape(REPS, TILES, TILE).astype(jnp.int32)


def draw_slot_counts(key, part):
    level_key, full_key = jax.random.split(key)
    levels = jax.random.randint(level_key, (REPS,), INSERT // 4, INSERT + 1)
    chosen = jax.random.randint(full_key, (), 0, REPS)
    return jnp.where(jnp.arange(REPS) == chosen, INSERT, levels).astype(jnp.int32)


def level_of(stream_key, dims, cuts, least, high):
    loudness = 1.0
    for axis_at, parts in cuts:
        heights = jax.random.uniform(jax.random.fold_in(jax.random.fold_in(stream_key, 6), axis_at), (parts,), jnp.float32, least / len(cuts), high / len(cuts))
        loudness = loudness * jnp.repeat(jnp.exp(heights), dims[axis_at] // parts).reshape((-1,) + (1,) * (len(dims) - 1 - axis_at))
    return loudness


def normal_values(own_key, shape, scale, reach, pieces=(), kind=jnp.bfloat16):
    array = scale * jax.random.normal(own_key, shape, jnp.float32)
    if pieces:
        array = array * level_of(own_key, shape, pieces, -0.22, 0.18)
    return jnp.clip(array, -reach, reach).astype(kind)


def setup_inputs(seed: int = 0) -> dict:
    streams_of = jax.random.split(jax.random.key(seed), 9)
    positions = jnp.clip(0.6 * jax.random.uniform(streams_of[0], (REPS, TILES, 3, TILE), jnp.float32) ** level_of(streams_of[0], (REPS, TILES, 3, TILE), ((0, 16), (1, 32)), -0.2, 0.2), 0.0, 0.6)
    velocities = draw_velocities(jax.random.fold_in(streams_of[8], 71), 0)
    strength = jnp.clip(0.5 + 1.0 * jax.random.uniform(streams_of[2], (REPS, TILES, TILE), jnp.float32) ** level_of(streams_of[2], (REPS, TILES, TILE), ((0, 16), (1, 32)), -0.2, 0.2), 0.5, 1.5)
    noise = draw_noise(jax.random.fold_in(streams_of[8], 71), 0)
    neighbours = draw_neighbours(jax.random.fold_in(streams_of[8], 71), 0)
    bins = draw_bins(jax.random.fold_in(streams_of[8], 71), 0)
    thermal = normal_values(streams_of[6], (REPS, 3, INSERT), 0.5, 3.0, ((0, 16),), jnp.float32)
    slot_counts = draw_slot_counts(jax.random.fold_in(streams_of[8], 71), 0)
    return {"positions": positions, "velocities": velocities, "strength": strength, "noise": noise, "neighbours": neighbours, "bins": bins, "thermal": thermal, "slot_counts": slot_counts}


TIME_STEP = 0.02
REPULSION = 0.25
FRICTION = 1.0
NOISE_AMP = 0.25
SPACING = 0.02
TARGET_FLOW = 1.0


def bead_forces(own_tile, partners, shift_x):
    offset_x = own_tile[0][None, :, None] - partners[:, 0][:, None, :] + shift_x[:, None, None]
    offset_y = own_tile[1][None, :, None] - partners[:, 1][:, None, :]
    offset_z = own_tile[2][None, :, None] - partners[:, 2][:, None, :]
    closing = offset_x * (own_tile[3][None, :, None] - partners[:, 3][:, None, :])
    closing = closing + offset_y * (own_tile[4][None, :, None] - partners[:, 4][:, None, :])
    closing = closing + offset_z * (own_tile[5][None, :, None] - partners[:, 5][:, None, :])
    weight = jnp.maximum(1.0 - (offset_x * offset_x + offset_y * offset_y + offset_z * offset_z), 0.0)
    kicks = own_tile[7][None, :, None] + partners[:, 7][:, None, :]
    factor = own_tile[6][None, :, None] * partners[:, 6][:, None, :] * weight
    factor = factor * (REPULSION - FRICTION * weight * closing + NOISE_AMP * kicks)
    return jnp.stack([jnp.sum(factor * offset_x, axis=(0, 2)), jnp.sum(factor * offset_y, axis=(0, 2)), jnp.sum(factor * offset_z, axis=(0, 2))])


def replica_forces(padded, rows):
    tiles = rows.shape[0]
    group = math.gcd(tiles, 64)
    width = padded.shape[-1]
    own_index = jnp.arange(tiles, dtype=jnp.int32) + HALO
    own_tiles = padded[HALO:HALO + tiles]

    def per_group(item):
        own_group, link_group, index_group = item
        partners = padded[link_group]
        shifts = SPACING * (index_group[:, None] - link_group).astype(jnp.float32)
        return jax.vmap(bead_forces)(own_group, partners, shifts)

    result = lax.map(per_group, (own_tiles.reshape(tiles // group, group, 8, width), rows.reshape(tiles // group, group, rows.shape[1]), own_index.reshape(tiles // group, group)))
    return result.reshape(tiles, 3, width)


def reference(positions, velocities, strength, noise, neighbours, bins, thermal, slot_counts):
    slab_of = (jnp.arange(TILES, dtype=jnp.int32) // TILES_DEV).astype(jnp.int32)
    partner_rows = (neighbours + (slab_of * TILES_DEV)[None, :, None]).astype(jnp.int32)
    for substep in range(SUBSTEPS):
        packed = jnp.concatenate([positions, velocities, strength[:, :, None, :], noise[substep][:, :, None, :]], axis=2)
        padded = jnp.pad(packed, ((0, 0), (HALO, HALO), (0, 0), (0, 0)))
        forces = lax.map(lambda item: replica_forces(item[0], item[1]), (padded, partner_rows))
        velocities = velocities + TIME_STEP * forces
        positions = positions + TIME_STEP * velocities
    slab_bins = (bins + (slab_of * BINS_DEV)[None, :, None]).astype(jnp.int32)
    values = jnp.transpose(velocities, (2, 0, 1, 3)).reshape(3, -1)
    labels = slab_bins.reshape(-1)
    momentum = jax.ops.segment_sum(values.T, labels, num_segments=BINS)
    counts = jax.ops.segment_sum(jnp.ones(labels.shape, jnp.float32), labels, num_segments=BINS)
    bin_velocity = (momentum / counts[:, None]).T
    flux = jnp.sum(velocities[:, :, 0, :]) / (REPS * TILES * TILE)
    inflow = 2.0 * TARGET_FLOW - flux
    live = jnp.arange(INSERT, dtype=jnp.int32)[None, :] < slot_counts[:, None]
    lift = jnp.where(jnp.arange(3)[:, None] == 0, inflow, jnp.float32(0.0))
    inserted = jnp.where(live[:, None, :], thermal + lift[None], jnp.float32(0.0))
    return positions, velocities, bin_velocity, inserted
```

```python
import jax
import jax.numpy as jnp
from jax import lax
from jax.sharding import PartitionSpec as P

HALO = 16
BINS_DEV = 1024


TIME_STEP = 0.02
REPULSION = 0.25
FRICTION = 1.0
NOISE_AMP = 0.25
SPACING = 0.02
TARGET_FLOW = 1.0


def padded(value, sides, width):
    for axis, dim in sides:
        count, length = (lax.axis_size(axis), value.shape[dim])
        up = [(i, (i + 1) % count) for i in range(count - 1)]
        down = [(j, i) for i, j in up]
        last = lax.slice_in_dim(value, length - width, length, axis=dim)
        initial = lax.slice_in_dim(value, 0, width, axis=dim)
        before = lax.ppermute(last, axis, up)
        after = lax.ppermute(initial, axis, down)
        value = jnp.concatenate([before, value, after], axis=dim)
    return value


def butterfly_sum(value, axis, radix=4):
    count = lax.axis_size(axis)
    stride = 1
    while stride < count:
        group = min(radix, count // stride)
        leaves = [value]
        for j in range(1, group):
            pairs = [(i, i ^ (j * stride)) for i in range(count)]
            leaves.append(lax.ppermute(value, axis, pairs))
        while len(leaves) > 1:
            leaves = [leaves[k] + leaves[k + 1] for k in range(0, len(leaves), 2)]
        value = leaves[0]
        stride *= group
    return value


def bead_forces(own_tile, partners, shift_x):
    offset_x = own_tile[0][None, :, None] - partners[:, 0][:, None, :] + shift_x[:, None, None]
    offset_y = own_tile[1][None, :, None] - partners[:, 1][:, None, :]
    offset_z = own_tile[2][None, :, None] - partners[:, 2][:, None, :]
    closing = offset_x * (own_tile[3][None, :, None] - partners[:, 3][:, None, :])
    closing = closing + offset_y * (own_tile[4][None, :, None] - partners[:, 4][:, None, :])
    closing = closing + offset_z * (own_tile[5][None, :, None] - partners[:, 5][:, None, :])
    weight = jnp.maximum(
        1.0 - (offset_x * offset_x + offset_y * offset_y + offset_z * offset_z), 0.0
    )
    kicks = own_tile[7][None, :, None] + partners[:, 7][:, None, :]
    factor = own_tile[6][None, :, None] * partners[:, 6][:, None, :] * weight
    factor = factor * (REPULSION - FRICTION * weight * closing + NOISE_AMP * kicks)
    return jnp.stack(
        [
            jnp.sum(factor * offset_x, axis=(0, 2)),
            jnp.sum(factor * offset_y, axis=(0, 2)),
            jnp.sum(factor * offset_z, axis=(0, 2)),
        ]
    )


def slab_forces(extended, links):
    tiles = links.shape[0]
    margin = (extended.shape[0] - tiles) // 2
    group = 8
    width = extended.shape[-1]
    own_index = jnp.arange(tiles, dtype=jnp.int32) + margin
    own_tiles = extended[margin : margin + tiles]

    def per_group(item):
        own_group, link_group, index_group = item
        partners = extended[link_group]
        shifts = SPACING * (index_group[:, None] - link_group).astype(jnp.float32)
        return jax.vmap(bead_forces)(own_group, partners, shifts)

    result = lax.map(
        per_group,
        (
            own_tiles.reshape(tiles // group, group, 8, width),
            links.reshape(tiles // group, group, links.shape[1]),
            own_index.reshape(tiles // group, group),
        ),
    )
    return result.reshape(tiles, 3, width)


def shards(positions, velocities, strength, noise, neighbours, bins, thermal, slot_counts):
    place = positions[0]
    speed = velocities[0]
    weights = strength[0]
    links = neighbours[0]
    substeps = noise.shape[0]
    for substep in range(substeps):
        packed = jnp.concatenate(
            [place, speed, weights[:, None, :], noise[substep, 0][:, None, :]], axis=1
        )
        extended = padded(packed, (("space", 0),), HALO)
        speed = speed + TIME_STEP * slab_forces(extended, links)
        place = place + TIME_STEP * speed
    tiles = speed.shape[0]
    width = speed.shape[-1]
    group = 8
    labels = jnp.arange(BINS_DEV, dtype=jnp.int32)
    grouped_speed = speed.reshape(tiles // group, group, 3, width)
    grouped_bins = bins[0].reshape(tiles // group, group * width)

    def accumulate(carry, item):
        momentum, counts = carry
        block_speed, block_bins = item
        table = (block_bins[:, None] == labels[None, :]).astype(jnp.float32)
        rows_now = jnp.transpose(block_speed, (1, 0, 2)).reshape(3, group * width)
        momentum = momentum + jnp.dot(
            rows_now, table, precision=lax.Precision.HIGHEST, preferred_element_type=jnp.float32
        )
        counts = counts + jnp.sum(table, axis=0)
        return ((momentum, counts), None)

    start = (jnp.zeros((3, BINS_DEV), jnp.float32), jnp.zeros((BINS_DEV,), jnp.float32))
    (momentum, counts), unused = lax.scan(accumulate, start, (grouped_speed, grouped_bins))
    local_flux = jnp.sum(speed[:, 0, :])
    packed = jnp.concatenate(
        [momentum, counts[None, :], jnp.full((4, BINS_DEV), local_flux, jnp.float32)], axis=0
    )
    packed = butterfly_sum(packed, "rep")
    momentum, counts = packed[0:3], packed[3]
    slab_flux = jnp.full((8, 128), packed[4, 0], jnp.float32)
    flux_sum = butterfly_sum(slab_flux, "space")[0, 0]
    bin_velocity = momentum / counts[None, :]
    total_beads = lax.axis_size("rep") * lax.axis_size("space") * tiles * width
    inflow = 2.0 * TARGET_FLOW - flux_sum / total_beads
    slots = jnp.arange(thermal.shape[-1], dtype=jnp.int32)
    live = slots[None, :] < slot_counts[:, None]
    lift = jnp.where(jnp.arange(3)[:, None] == 0, inflow, jnp.float32(0.0))
    inserted = jnp.where(live[:, None, :], thermal + lift[None], jnp.float32(0.0))
    return (place[None], speed[None], bin_velocity, inserted)


def solution(mesh):
    return jax.shard_map(
        shards,
        mesh=mesh,
        in_specs=(
            P("rep", "space", None, None),
            P("rep", "space", None, None),
            P("rep", "space", None),
            P(None, "rep", "space", None),
            P("rep", "space", None),
            P("rep", "space", None),
            P("rep", None, None),
            P("rep"),
        ),
        out_specs=(
            P("rep", "space", None, None),
            P("rep", "space", None, None),
            P(None, "space"),
            P("rep", None, None),
        ),
        check_vma=False,
    )
```

```python
import functools

import jax
import jax.numpy as jnp
from jax import lax
from jax.experimental import pallas as pl
from jax.experimental.pallas import tpu as pltpu
from jax.sharding import PartitionSpec as P

HALO = 16
BINS_DEV = 1024


TIME_STEP = 0.02
REPULSION = 0.25
FRICTION = 1.0
NOISE_AMP = 0.25
SPACING = 0.02
TARGET_FLOW = 1.0


def butterfly_sum(value, axis, radix=4):
    count = lax.axis_size(axis)
    stride = 1
    while stride < count:
        group = min(radix, count // stride)
        leaves = [value]
        for j in range(1, group):
            pairs = [(i, i ^ (j * stride)) for i in range(count)]
            leaves.append(lax.ppermute(value, axis, pairs))
        while len(leaves) > 1:
            leaves = [leaves[k] + leaves[k + 1] for k in range(0, len(leaves), 2)]
        value = leaves[0]
        stride *= group
    return value


def force_kernel(links_ref, shifts_ref, src_ref, pos_ref, vel_ref, *, first, count, skip, origin, links):
    width = src_ref.shape[-1]
    rows = 8

    def tile(i, carry):
        t = first + i + jnp.where(i >= count // 2, skip, 0)
        own = src_ref[t + HALO - origin]
        own_rows = [jnp.broadcast_to(own[f : f + 1, :], (rows, width)) for f in range(6)]
        kick_a = jnp.broadcast_to(REPULSION + NOISE_AMP * own[7:8, :], (rows, width))
        acc = [jnp.zeros((rows, width), jnp.float32) for _ in range(3)]
        for link in range(links):
            p = links_ref[t * links + link] - origin
            shift = shifts_ref[t * links + link]
            part = src_ref[p]
            fields = [part[0:1, :] - shift] + [part[f : f + 1, :] for f in range(1, 7)]
            fields.append(NOISE_AMP * part[7:8, :])
            spread = [jnp.broadcast_to(v, (rows, width)) for v in fields]
            for j in range(width // rows):
                xb, yb, zb, ub, vb, wb, sb, hb = [
                    pltpu.roll(v, rows * j, 1, stride=1, stride_axis=0) for v in spread
                ]
                dx = own_rows[0] - xb
                dy = own_rows[1] - yb
                dz = own_rows[2] - zb
                closing = dx * (own_rows[3] - ub) + dy * (own_rows[4] - vb) + dz * (own_rows[5] - wb)
                weight = jnp.maximum(1.0 - (dx * dx + dy * dy + dz * dz), 0.0)
                factor = sb * weight * (kick_a + hb - FRICTION * weight * closing)
                acc[0] = acc[0] + factor * dx
                acc[1] = acc[1] + factor * dy
                acc[2] = acc[2] + factor * dz
        strength_a = own[6:7, :]
        force = jnp.concatenate([strength_a * jnp.sum(a, axis=0, keepdims=True) for a in acc], axis=0)
        speed = own[3:6, :] + TIME_STEP * force
        vel_ref[t] = speed
        pos_ref[t] = own[0:3, :] + TIME_STEP * speed
        return carry

    lax.fori_loop(0, count, tile, 0)


def substep_call(links, shifts, src, carry_out, *, first, count, skip, origin, tiles):
    per_tile = links.shape[0] // tiles
    width = src.shape[-1]
    kernel = functools.partial(force_kernel, first=first, count=count, skip=skip, origin=origin, links=per_tile)
    out_shape = (
        jax.ShapeDtypeStruct((tiles, 3, width), jnp.float32),
        jax.ShapeDtypeStruct((tiles, 3, width), jnp.float32),
    )
    pairs = count * per_tile * width * width
    in_specs = [
        pl.BlockSpec(memory_space=pltpu.SMEM),
        pl.BlockSpec(memory_space=pltpu.SMEM),
        pl.BlockSpec(memory_space=pltpu.VMEM),
    ]
    args = [links, shifts, src]
    if carry_out is not None:
        in_specs += [pl.BlockSpec(memory_space=pltpu.VMEM)] * 2
        args += list(carry_out)
        keep = slice(count // 2, tiles - count // 2)

        def body(l, s, x, p_in, v_in, p_out, v_out):
            p_out[keep] = p_in[keep]
            v_out[keep] = v_in[keep]
            kernel(l, s, x, p_out, v_out)
    else:
        body = kernel
    return pl.pallas_call(
        body,
        out_shape=out_shape,
        in_specs=in_specs,
        out_specs=(pl.BlockSpec(memory_space=pltpu.VMEM), pl.BlockSpec(memory_space=pltpu.VMEM)),
        cost_estimate=pl.CostEstimate(flops=30 * pairs, transcendentals=0, bytes_accessed=src.size * 4),
    )(*args)


def shards(positions, velocities, strength, noise, neighbours, bins, thermal, slot_counts):
    place = positions[0]
    speed = velocities[0]
    weights = strength[0]
    links = neighbours[0]
    substeps = noise.shape[0]
    tiles = links.shape[0]
    count = lax.axis_size("space")
    up = [(i, i + 1) for i in range(count - 1)]
    down = [(i + 1, i) for i in range(count - 1)]
    own_index = jnp.arange(tiles, dtype=jnp.int32)[:, None] + HALO
    shifts = (SPACING * (own_index - links).astype(jnp.float32)).reshape(-1)
    flat_links = links.reshape(-1)
    edge = tiles - 2 * HALO
    for substep in range(substeps):
        packed = jnp.concatenate(
            [place, speed, weights[:, None, :], noise[substep, 0][:, None, :]], axis=1
        )
        before = lax.ppermute(packed[tiles - HALO :], "space", up)
        after = lax.ppermute(packed[:HALO], "space", down)
        inner = substep_call(
            flat_links, shifts, packed, None, first=HALO, count=edge, skip=0, origin=HALO, tiles=tiles
        )
        extended = jnp.concatenate([before, packed, after], axis=0)
        place, speed = substep_call(
            flat_links, shifts, extended, inner, first=0, count=2 * HALO, skip=edge, origin=0, tiles=tiles
        )
    tiles = speed.shape[0]
    width = speed.shape[-1]
    group = 8
    labels = jnp.arange(BINS_DEV, dtype=jnp.int32)
    grouped_speed = speed.reshape(tiles // group, group, 3, width)
    grouped_bins = bins[0].reshape(tiles // group, group * width)

    def accumulate(carry, item):
        momentum, counts = carry
        block_speed, block_bins = item
        table = (block_bins[:, None] == labels[None, :]).astype(jnp.float32)
        rows_now = jnp.transpose(block_speed, (1, 0, 2)).reshape(3, group * width)
        momentum = momentum + jnp.dot(
            rows_now, table, precision=lax.Precision.HIGHEST, preferred_element_type=jnp.float32
        )
        counts = counts + jnp.sum(table, axis=0)
        return ((momentum, counts), None)

    start = (jnp.zeros((3, BINS_DEV), jnp.float32), jnp.zeros((BINS_DEV,), jnp.float32))
    (momentum, counts), unused = lax.scan(accumulate, start, (grouped_speed, grouped_bins))
    local_flux = jnp.sum(speed[:, 0, :])
    packed = jnp.concatenate(
        [momentum, counts[None, :], jnp.full((4, BINS_DEV), local_flux, jnp.float32)], axis=0
    )
    packed = butterfly_sum(packed, "rep")
    momentum, counts = packed[0:3], packed[3]
    slab_flux = jnp.full((8, 128), packed[4, 0], jnp.float32)
    flux_sum = butterfly_sum(slab_flux, "space")[0, 0]
    bin_velocity = momentum / counts[None, :]
    total_beads = lax.axis_size("rep") * lax.axis_size("space") * tiles * width
    inflow = 2.0 * TARGET_FLOW - flux_sum / total_beads
    slots = jnp.arange(thermal.shape[-1], dtype=jnp.int32)
    live = slots[None, :] < slot_counts[:, None]
    lift = jnp.where(jnp.arange(3)[:, None] == 0, inflow, jnp.float32(0.0))
    inserted = jnp.where(live[:, None, :], thermal + lift[None], jnp.float32(0.0))
    return (place[None], speed[None], bin_velocity, inserted)


def solution(mesh):
    return jax.shard_map(
        shards,
        mesh=mesh,
        in_specs=(
            P("rep", "space", None, None),
            P("rep", "space", None, None),
            P("rep", "space", None),
            P(None, "rep", "space", None),
            P("rep", "space", None),
            P("rep", "space", None),
            P("rep", None, None),
            P("rep"),
        ),
        out_specs=(
            P("rep", "space", None, None),
            P("rep", "space", None, None),
            P(None, "space"),
            P("rep", None, None),
        ),
        check_vma=False,
    )
```

```python
import jax
import jax.numpy as jnp
from jax import lax
from jax.sharding import PartitionSpec as P

HALO = 16
BINS_DEV = 1024


TIME_STEP = 0.02
REPULSION = 0.25
FRICTION = 1.0
NOISE_AMP = 0.25
SPACING = 0.02
TARGET_FLOW = 1.0


def padded(value, sides, width):
    for axis, dim in sides:
        count, length = (lax.axis_size(axis), value.shape[dim])
        up = [(i, (i + 1) % count) for i in range(count - 1)]
        down = [(j, i) for i, j in up]
        last = lax.slice_in_dim(value, length - width, length, axis=dim)
        initial = lax.slice_in_dim(value, 0, width, axis=dim)
        before = lax.ppermute(last, axis, up)
        after = lax.ppermute(initial, axis, down)
        value = jnp.concatenate([before, value, after], axis=dim)
    return value


def butterfly_sum(value, axis, radix=2):
    count = lax.axis_size(axis)
    stride = 1
    while stride < count:
        group = min(radix, count // stride)
        leaves = [value]
        for j in range(1, group):
            pairs = [(i, i ^ (j * stride)) for i in range(count)]
            leaves.append(lax.ppermute(value, axis, pairs))
        while len(leaves) > 1:
            leaves = [leaves[k] + leaves[k + 1] for k in range(0, len(leaves), 2)]
        value = leaves[0]
        stride *= group
    return value


def bead_forces(own_tile, partners, shift_x):
    offset_x = own_tile[0][None, :, None] - partners[:, 0][:, None, :] + shift_x[:, None, None]
    offset_y = own_tile[1][None, :, None] - partners[:, 1][:, None, :]
    offset_z = own_tile[2][None, :, None] - partners[:, 2][:, None, :]
    closing = offset_x * (own_tile[3][None, :, None] - partners[:, 3][:, None, :])
    closing = closing + offset_y * (own_tile[4][None, :, None] - partners[:, 4][:, None, :])
    closing = closing + offset_z * (own_tile[5][None, :, None] - partners[:, 5][:, None, :])
    weight = jnp.maximum(
        1.0 - (offset_x * offset_x + offset_y * offset_y + offset_z * offset_z), 0.0
    )
    kicks = own_tile[7][None, :, None] + partners[:, 7][:, None, :]
    factor = own_tile[6][None, :, None] * partners[:, 6][:, None, :] * weight
    factor = factor * (REPULSION - FRICTION * weight * closing + NOISE_AMP * kicks)
    return jnp.stack(
        [
            jnp.sum(factor * offset_x, axis=(0, 2)),
            jnp.sum(factor * offset_y, axis=(0, 2)),
            jnp.sum(factor * offset_z, axis=(0, 2)),
        ]
    )


def slab_forces(extended, links):
    tiles = links.shape[0]
    margin = (extended.shape[0] - tiles) // 2
    group = 8
    width = extended.shape[-1]
    own_index = jnp.arange(tiles, dtype=jnp.int32) + margin
    own_tiles = extended[margin : margin + tiles]

    def per_group(item):
        own_group, link_group, index_group = item
        partners = extended[link_group]
        shifts = SPACING * (index_group[:, None] - link_group).astype(jnp.float32)
        return jax.vmap(bead_forces)(own_group, partners, shifts)

    result = lax.map(
        per_group,
        (
            own_tiles.reshape(tiles // group, group, 8, width),
            links.reshape(tiles // group, group, links.shape[1]),
            own_index.reshape(tiles // group, group),
        ),
    )
    return result.reshape(tiles, 3, width)


def shards(positions, velocities, strength, noise, neighbours, bins, thermal, slot_counts):
    place = positions[0]
    speed = velocities[0]
    weights = strength[0]
    links = neighbours[0]
    substeps = noise.shape[0]
    for substep in range(substeps):
        packed = jnp.concatenate(
            [place, speed, weights[:, None, :], noise[substep, 0][:, None, :]], axis=1
        )
        extended = padded(packed, (("space", 0),), HALO)
        speed = speed + TIME_STEP * slab_forces(extended, links)
        place = place + TIME_STEP * speed
    tiles = speed.shape[0]
    width = speed.shape[-1]
    group = 8
    labels = jnp.arange(BINS_DEV, dtype=jnp.int32)
    grouped_speed = speed.reshape(tiles // group, group, 3, width)
    grouped_bins = bins[0].reshape(tiles // group, group * width)

    def accumulate(carry, item):
        momentum, counts = carry
        block_speed, block_bins = item
        table = (block_bins[:, None] == labels[None, :]).astype(jnp.float32)
        rows_now = jnp.transpose(block_speed, (1, 0, 2)).reshape(3, group * width)
        momentum = momentum + jnp.dot(
            rows_now, table, precision=lax.Precision.HIGHEST, preferred_element_type=jnp.float32
        )
        counts = counts + jnp.sum(table, axis=0)
        return ((momentum, counts), None)

    start = (jnp.zeros((3, BINS_DEV), jnp.float32), jnp.zeros((BINS_DEV,), jnp.float32))
    (momentum, counts), unused = lax.scan(accumulate, start, (grouped_speed, grouped_bins))
    local_flux = jnp.sum(speed[:, 0, :])
    packed = jnp.concatenate(
        [momentum, counts[None, :], jnp.full((4, BINS_DEV), local_flux, jnp.float32)], axis=0
    )
    packed = butterfly_sum(packed, "rep")
    momentum, counts = packed[0:3], packed[3]
    slab_flux = jnp.full((8, 128), packed[4, 0], jnp.float32)
    flux_sum = butterfly_sum(slab_flux, "space")[0, 0]
    bin_velocity = momentum / counts[None, :]
    total_beads = lax.axis_size("rep") * lax.axis_size("space") * tiles * width
    inflow = 2.0 * TARGET_FLOW - flux_sum / total_beads
    slots = jnp.arange(thermal.shape[-1], dtype=jnp.int32)
    live = slots[None, :] < slot_counts[:, None]
    lift = jnp.where(jnp.arange(3)[:, None] == 0, inflow, jnp.float32(0.0))
    inserted = jnp.where(live[:, None, :], thermal + lift[None], jnp.float32(0.0))
    return (place[None], speed[None], bin_velocity, inserted)


def solution(mesh):
    return jax.shard_map(
        shards,
        mesh=mesh,
        in_specs=(
            P("rep", "space", None, None),
            P("rep", "space", None, None),
            P("rep", "space", None),
            P(None, "rep", "space", None),
            P("rep", "space", None),
            P("rep", "space", None),
            P("rep", None, None),
            P("rep"),
        ),
        out_specs=(
            P("rep", "space", None, None),
            P("rep", "space", None, None),
            P(None, "space"),
            P("rep", None, None),
        ),
        check_vma=False,
    )
```

```python
import jax
import jax.numpy as jnp
from jax import lax
from jax.sharding import PartitionSpec as P

HALO = 16
BINS_DEV = 1024


TIME_STEP = 0.02
REPULSION = 0.25
FRICTION = 1.0
NOISE_AMP = 0.25
SPACING = 0.02
TARGET_FLOW = 1.0


def padded(value, sides, width):
    for axis, dim in sides:
        count, length = (lax.axis_size(axis), value.shape[dim])
        up = [(i, (i + 1) % count) for i in range(count - 1)]
        down = [(j, i) for i, j in up]
        last = lax.slice_in_dim(value, length - width, length, axis=dim)
        initial = lax.slice_in_dim(value, 0, width, axis=dim)
        before = lax.ppermute(last, axis, up)
        after = lax.ppermute(initial, axis, down)
        value = jnp.concatenate([before, value, after], axis=dim)
    return value


def butterfly_sum(value, axis, radix=2):
    count = lax.axis_size(axis)
    stride = 1
    while stride < count:
        group = min(radix, count // stride)
        leaves = [value]
        for j in range(1, group):
            pairs = [(i, i ^ (j * stride)) for i in range(count)]
            leaves.append(lax.ppermute(value, axis, pairs))
        while len(leaves) > 1:
            leaves = [leaves[k] + leaves[k + 1] for k in range(0, len(leaves), 2)]
        value = leaves[0]
        stride *= group
    return value


def bead_forces(own_tile, partners, shift_x):
    offset_x = own_tile[0][None, :, None] - partners[:, 0][:, None, :] + shift_x[:, None, None]
    offset_y = own_tile[1][None, :, None] - partners[:, 1][:, None, :]
    offset_z = own_tile[2][None, :, None] - partners[:, 2][:, None, :]
    closing = offset_x * (own_tile[3][None, :, None] - partners[:, 3][:, None, :])
    closing = closing + offset_y * (own_tile[4][None, :, None] - partners[:, 4][:, None, :])
    closing = closing + offset_z * (own_tile[5][None, :, None] - partners[:, 5][:, None, :])
    weight = jnp.maximum(
        1.0 - (offset_x * offset_x + offset_y * offset_y + offset_z * offset_z), 0.0
    )
    kicks = own_tile[7][None, :, None] + partners[:, 7][:, None, :]
    factor = own_tile[6][None, :, None] * partners[:, 6][:, None, :] * weight
    factor = factor * (REPULSION - FRICTION * weight * closing + NOISE_AMP * kicks)
    return jnp.stack(
        [
            jnp.sum(factor * offset_x, axis=(0, 2)),
            jnp.sum(factor * offset_y, axis=(0, 2)),
            jnp.sum(factor * offset_z, axis=(0, 2)),
        ]
    )


def tile_forces(source, own_index, link_index):
    tiles = own_index.shape[0]
    group = 8
    width = source.shape[-1]
    own_tiles = source[own_index]

    def per_group(item):
        own_group, link_group, index_group = item
        partners = source[link_group]
        shifts = SPACING * (index_group[:, None] - link_group).astype(jnp.float32)
        return jax.vmap(bead_forces)(own_group, partners, shifts)

    result = lax.map(
        per_group,
        (
            own_tiles.reshape(tiles // group, group, 8, width),
            link_index.reshape(tiles // group, group, link_index.shape[1]),
            own_index.reshape(tiles // group, group),
        ),
    )
    return result.reshape(tiles, 3, width)


def shards(positions, velocities, strength, noise, neighbours, bins, thermal, slot_counts):
    place = positions[0]
    speed = velocities[0]
    weights = strength[0]
    links = neighbours[0]
    substeps = noise.shape[0]
    tiles = links.shape[0]
    count = lax.axis_size("space")
    up = [(i, i + 1) for i in range(count - 1)]
    down = [(i + 1, i) for i in range(count - 1)]
    local = jnp.arange(tiles, dtype=jnp.int32)
    inner = local[HALO : tiles - HALO]
    outer = jnp.concatenate([local[:HALO], local[tiles - HALO :]])
    inner_links = links[HALO : tiles - HALO] - HALO
    outer_links = jnp.concatenate([links[:HALO], links[tiles - HALO :]], axis=0)
    for substep in range(substeps):
        packed = jnp.concatenate(
            [place, speed, weights[:, None, :], noise[substep, 0][:, None, :]], axis=1
        )
        before = lax.ppermute(packed[tiles - HALO :], "space", up)
        after = lax.ppermute(packed[:HALO], "space", down)
        inner_force = tile_forces(packed, inner, inner_links)
        extended = jnp.concatenate([before, packed, after], axis=0)
        outer_force = tile_forces(extended, outer + HALO, outer_links)
        force = jnp.concatenate(
            [outer_force[:HALO], inner_force, outer_force[HALO:]], axis=0
        )
        speed = speed + TIME_STEP * force
        place = place + TIME_STEP * speed
    tiles = speed.shape[0]
    width = speed.shape[-1]
    group = 8
    labels = jnp.arange(BINS_DEV, dtype=jnp.int32)
    grouped_speed = speed.reshape(tiles // group, group, 3, width)
    grouped_bins = bins[0].reshape(tiles // group, group * width)

    def accumulate(carry, item):
        momentum, counts = carry
        block_speed, block_bins = item
        table = (block_bins[:, None] == labels[None, :]).astype(jnp.float32)
        rows_now = jnp.transpose(block_speed, (1, 0, 2)).reshape(3, group * width)
        momentum = momentum + jnp.dot(
            rows_now, table, precision=lax.Precision.HIGHEST, preferred_element_type=jnp.float32
        )
        counts = counts + jnp.sum(table, axis=0)
        return ((momentum, counts), None)

    start = (jnp.zeros((3, BINS_DEV), jnp.float32), jnp.zeros((BINS_DEV,), jnp.float32))
    (momentum, counts), unused = lax.scan(accumulate, start, (grouped_speed, grouped_bins))
    local_flux = jnp.sum(speed[:, 0, :])
    packed = jnp.concatenate(
        [momentum, counts[None, :], jnp.full((4, BINS_DEV), local_flux, jnp.float32)], axis=0
    )
    packed = butterfly_sum(packed, "rep")
    momentum, counts = packed[0:3], packed[3]
    slab_flux = jnp.full((8, 128), packed[4, 0], jnp.float32)
    flux_sum = butterfly_sum(slab_flux, "space")[0, 0]
    bin_velocity = momentum / counts[None, :]
    total_beads = lax.axis_size("rep") * lax.axis_size("space") * tiles * width
    inflow = 2.0 * TARGET_FLOW - flux_sum / total_beads
    slots = jnp.arange(thermal.shape[-1], dtype=jnp.int32)
    live = slots[None, :] < slot_counts[:, None]
    lift = jnp.where(jnp.arange(3)[:, None] == 0, inflow, jnp.float32(0.0))
    inserted = jnp.where(live[:, None, :], thermal + lift[None], jnp.float32(0.0))
    return (place[None], speed[None], bin_velocity, inserted)


def solution(mesh):
    return jax.shard_map(
        shards,
        mesh=mesh,
        in_specs=(
            P("rep", "space", None, None),
            P("rep", "space", None, None),
            P("rep", "space", None),
            P(None, "rep", "space", None),
            P("rep", "space", None),
            P("rep", "space", None),
            P("rep", None, None),
            P("rep"),
        ),
        out_specs=(
            P("rep", "space", None, None),
            P("rep", "space", None, None),
            P(None, "space"),
            P("rep", None, None),
        ),
        check_vma=False,
    )
```

```python
import jax
import jax.numpy as jnp
from jax import lax
from jax.sharding import PartitionSpec as P

HALO = 16
BINS_DEV = 1024


TIME_STEP = 0.02
REPULSION = 0.25
FRICTION = 1.0
NOISE_AMP = 0.25
SPACING = 0.02
TARGET_FLOW = 1.0


def padded(value, sides, width):
    for axis, dim in sides:
        count, length = (lax.axis_size(axis), value.shape[dim])
        up = [(i, (i + 1) % count) for i in range(count - 1)]
        down = [(j, i) for i, j in up]
        last = lax.slice_in_dim(value, length - width, length, axis=dim)
        initial = lax.slice_in_dim(value, 0, width, axis=dim)
        before = lax.ppermute(last, axis, up)
        after = lax.ppermute(initial, axis, down)
        value = jnp.concatenate([before, value, after], axis=dim)
    return value


def butterfly_sum(value, axis, radix=2):
    count = lax.axis_size(axis)
    stride = 1
    while stride < count:
        group = min(radix, count // stride)
        leaves = [value]
        for j in range(1, group):
            pairs = [(i, i ^ (j * stride)) for i in range(count)]
            leaves.append(lax.ppermute(value, axis, pairs))
        while len(leaves) > 1:
            leaves = [leaves[k] + leaves[k + 1] for k in range(0, len(leaves), 2)]
        value = leaves[0]
        stride *= group
    return value


def bead_forces(own_tile, partners, shift_x):
    offset_x = own_tile[0][None, :, None] - partners[:, 0][:, None, :] + shift_x[:, None, None]
    offset_y = own_tile[1][None, :, None] - partners[:, 1][:, None, :]
    offset_z = own_tile[2][None, :, None] - partners[:, 2][:, None, :]
    closing = offset_x * (own_tile[3][None, :, None] - partners[:, 3][:, None, :])
    closing = closing + offset_y * (own_tile[4][None, :, None] - partners[:, 4][:, None, :])
    closing = closing + offset_z * (own_tile[5][None, :, None] - partners[:, 5][:, None, :])
    weight = jnp.maximum(
        1.0 - (offset_x * offset_x + offset_y * offset_y + offset_z * offset_z), 0.0
    )
    kicks = own_tile[7][None, :, None] + partners[:, 7][:, None, :]
    factor = own_tile[6][None, :, None] * partners[:, 6][:, None, :] * weight
    factor = factor * (REPULSION - FRICTION * weight * closing + NOISE_AMP * kicks)
    return jnp.stack(
        [
            jnp.sum(factor * offset_x, axis=(0, 2)),
            jnp.sum(factor * offset_y, axis=(0, 2)),
            jnp.sum(factor * offset_z, axis=(0, 2)),
        ]
    )


def tile_forces(source, own_index, link_index):
    tiles = own_index.shape[0]
    group = 8
    width = source.shape[-1]
    own_tiles = source[own_index]

    def per_group(item):
        own_group, link_group, index_group = item
        partners = source[link_group]
        shifts = SPACING * (index_group[:, None] - link_group).astype(jnp.float32)
        return jax.vmap(bead_forces)(own_group, partners, shifts)

    result = lax.map(
        per_group,
        (
            own_tiles.reshape(tiles // group, group, 8, width),
            link_index.reshape(tiles // group, group, link_index.shape[1]),
            own_index.reshape(tiles // group, group),
        ),
    )
    return result.reshape(tiles, 3, width)


def shards(positions, velocities, strength, noise, neighbours, bins, thermal, slot_counts):
    place = positions[0]
    speed = velocities[0]
    weights = strength[0]
    links = neighbours[0]
    substeps = noise.shape[0]
    tiles = links.shape[0]
    count = lax.axis_size("space")
    up = [(i, i + 1) for i in range(count - 1)]
    down = [(i + 1, i) for i in range(count - 1)]
    local = jnp.arange(tiles, dtype=jnp.int32)
    inner = local[HALO : tiles - HALO]
    outer = jnp.concatenate([local[:HALO], local[tiles - HALO :]])
    inner_links = links[HALO : tiles - HALO] - HALO
    outer_links = jnp.concatenate([links[:HALO], links[tiles - HALO :]], axis=0)
    for substep in range(substeps):
        packed = jnp.concatenate(
            [place, speed, weights[:, None, :], noise[substep, 0][:, None, :]], axis=1
        )
        before = lax.ppermute(packed[tiles - HALO :], "space", up)
        after = lax.ppermute(packed[:HALO], "space", down)
        inner_force = tile_forces(packed, inner, inner_links)
        extended = jnp.concatenate([before, packed, after], axis=0)
        outer_force = tile_forces(extended, outer + HALO, outer_links)
        force = jnp.concatenate(
            [outer_force[:HALO], inner_force, outer_force[HALO:]], axis=0
        )
        speed = speed + TIME_STEP * force
        place = place + TIME_STEP * speed
    tiles = speed.shape[0]
    width = speed.shape[-1]
    group = 8
    labels = jnp.arange(BINS_DEV, dtype=jnp.int32)
    grouped_speed = speed.reshape(tiles // group, group, 3, width)
    grouped_bins = bins[0].reshape(tiles // group, group * width)

    def accumulate(carry, item):
        momentum, counts = carry
        block_speed, block_bins = item
        table = (block_bins[:, None] == labels[None, :]).astype(jnp.float32)
        rows_now = jnp.transpose(block_speed, (1, 0, 2)).reshape(3, group * width)
        momentum = momentum + jnp.dot(
            rows_now, table, precision=lax.Precision.HIGHEST, preferred_element_type=jnp.float32
        )
        counts = counts + jnp.sum(table, axis=0)
        return ((momentum, counts), None)

    local_flux = jnp.sum(speed[:, 0, :])
    slab_flux = butterfly_sum(jnp.full((8, 128), local_flux, jnp.float32), "space")
    start = (jnp.zeros((3, BINS_DEV), jnp.float32), jnp.zeros((BINS_DEV,), jnp.float32))
    chunks = 4
    steps = tiles // group // chunks
    momentum, counts = start
    for chunk in range(chunks):
        piece = slice(chunk * steps, (chunk + 1) * steps)
        (part_momentum, part_counts), unused = lax.scan(
            accumulate, start, (grouped_speed[piece], grouped_bins[piece])
        )
        momentum = momentum + part_momentum
        counts = counts + part_counts
    packed = jnp.concatenate(
        [momentum, counts[None, :], jnp.full((4, BINS_DEV), slab_flux[0, 0], jnp.float32)], axis=0
    )
    packed = butterfly_sum(packed, "rep")
    momentum, counts = packed[0:3], packed[3]
    flux_sum = packed[4, 0]
    bin_velocity = momentum / counts[None, :]
    total_beads = lax.axis_size("rep") * lax.axis_size("space") * tiles * width
    inflow = 2.0 * TARGET_FLOW - flux_sum / total_beads
    slots = jnp.arange(thermal.shape[-1], dtype=jnp.int32)
    live = slots[None, :] < slot_counts[:, None]
    lift = jnp.where(jnp.arange(3)[:, None] == 0, inflow, jnp.float32(0.0))
    inserted = jnp.where(live[:, None, :], thermal + lift[None], jnp.float32(0.0))
    return (place[None], speed[None], bin_velocity, inserted)


def solution(mesh):
    return jax.shard_map(
        shards,
        mesh=mesh,
        in_specs=(
            P("rep", "space", None, None),
            P("rep", "space", None, None),
            P("rep", "space", None),
            P(None, "rep", "space", None),
            P("rep", "space", None),
            P("rep", "space", None),
            P("rep", None, None),
            P("rep"),
        ),
        out_specs=(
            P("rep", "space", None, None),
            P("rep", "space", None, None),
            P(None, "space"),
            P("rep", None, None),
        ),
        check_vma=False,
    )
```

```python
import jax
import jax.numpy as jnp
from jax import lax
from jax.sharding import PartitionSpec as P

HALO = 16
BINS_DEV = 1024


TIME_STEP = 0.02
REPULSION = 0.25
FRICTION = 1.0
NOISE_AMP = 0.25
SPACING = 0.02
TARGET_FLOW = 1.0


def padded(value, sides, width):
    for axis, dim in sides:
        count, length = (lax.axis_size(axis), value.shape[dim])
        up = [(i, (i + 1) % count) for i in range(count - 1)]
        down = [(j, i) for i, j in up]
        last = lax.slice_in_dim(value, length - width, length, axis=dim)
        initial = lax.slice_in_dim(value, 0, width, axis=dim)
        before = lax.ppermute(last, axis, up)
        after = lax.ppermute(initial, axis, down)
        value = jnp.concatenate([before, value, after], axis=dim)
    return value


def butterfly_sum(value, axis, radix=2):
    count = lax.axis_size(axis)
    stride = 1
    while stride < count:
        group = min(radix, count // stride)
        leaves = [value]
        for j in range(1, group):
            pairs = [(i, i ^ (j * stride)) for i in range(count)]
            leaves.append(lax.ppermute(value, axis, pairs))
        while len(leaves) > 1:
            leaves = [leaves[k] + leaves[k + 1] for k in range(0, len(leaves), 2)]
        value = leaves[0]
        stride *= group
    return value


def bead_forces(own_tile, partners, shift_x):
    offset_x = own_tile[0][None, :, None] - partners[:, 0][:, None, :] + shift_x[:, None, None]
    offset_y = own_tile[1][None, :, None] - partners[:, 1][:, None, :]
    offset_z = own_tile[2][None, :, None] - partners[:, 2][:, None, :]
    closing = offset_x * (own_tile[3][None, :, None] - partners[:, 3][:, None, :])
    closing = closing + offset_y * (own_tile[4][None, :, None] - partners[:, 4][:, None, :])
    closing = closing + offset_z * (own_tile[5][None, :, None] - partners[:, 5][:, None, :])
    weight = jnp.maximum(
        1.0 - (offset_x * offset_x + offset_y * offset_y + offset_z * offset_z), 0.0
    )
    kicks = own_tile[7][None, :, None] + partners[:, 7][:, None, :]
    factor = own_tile[6][None, :, None] * partners[:, 6][:, None, :] * weight
    factor = factor * (REPULSION - FRICTION * weight * closing + NOISE_AMP * kicks)
    return jnp.stack(
        [
            jnp.sum(factor * offset_x, axis=(0, 2)),
            jnp.sum(factor * offset_y, axis=(0, 2)),
            jnp.sum(factor * offset_z, axis=(0, 2)),
        ]
    )


def tile_forces(source, own_index, link_index):
    tiles = own_index.shape[0]
    group = 32
    width = source.shape[-1]
    own_tiles = source[own_index]

    def per_group(item):
        own_group, link_group, index_group = item
        partners = source[link_group]
        shifts = SPACING * (index_group[:, None] - link_group).astype(jnp.float32)
        return jax.vmap(bead_forces)(own_group, partners, shifts)

    result = lax.map(
        per_group,
        (
            own_tiles.reshape(tiles // group, group, 8, width),
            link_index.reshape(tiles // group, group, link_index.shape[1]),
            own_index.reshape(tiles // group, group),
        ),
    )
    return result.reshape(tiles, 3, width)


def shards(positions, velocities, strength, noise, neighbours, bins, thermal, slot_counts):
    place = positions[0]
    speed = velocities[0]
    weights = strength[0]
    links = neighbours[0]
    substeps = noise.shape[0]
    tiles = links.shape[0]
    count = lax.axis_size("space")
    up = [(i, i + 1) for i in range(count - 1)]
    down = [(i + 1, i) for i in range(count - 1)]
    local = jnp.arange(tiles, dtype=jnp.int32)
    inner = local[HALO : tiles - HALO]
    outer = jnp.concatenate([local[:HALO], local[tiles - HALO :]])
    inner_links = links[HALO : tiles - HALO] - HALO
    outer_links = jnp.concatenate([links[:HALO], links[tiles - HALO :]], axis=0)
    for substep in range(substeps):
        packed = jnp.concatenate(
            [place, speed, weights[:, None, :], noise[substep, 0][:, None, :]], axis=1
        )
        before = lax.ppermute(packed[tiles - HALO :], "space", up)
        after = lax.ppermute(packed[:HALO], "space", down)
        inner_force = tile_forces(packed, inner, inner_links)
        extended = jnp.concatenate([before, packed, after], axis=0)
        outer_force = tile_forces(extended, outer + HALO, outer_links)
        force = jnp.concatenate(
            [outer_force[:HALO], inner_force, outer_force[HALO:]], axis=0
        )
        speed = speed + TIME_STEP * force
        place = place + TIME_STEP * speed
    tiles = speed.shape[0]
    width = speed.shape[-1]
    group = 8
    labels = jnp.arange(BINS_DEV, dtype=jnp.int32)
    grouped_speed = speed.reshape(tiles // group, group, 3, width)
    grouped_bins = bins[0].reshape(tiles // group, group * width)

    def accumulate(carry, item):
        momentum, counts = carry
        block_speed, block_bins = item
        table = (block_bins[:, None] == labels[None, :]).astype(jnp.float32)
        rows_now = jnp.transpose(block_speed, (1, 0, 2)).reshape(3, group * width)
        momentum = momentum + jnp.dot(
            rows_now, table, precision=lax.Precision.HIGHEST, preferred_element_type=jnp.float32
        )
        counts = counts + jnp.sum(table, axis=0)
        return ((momentum, counts), None)

    local_flux = jnp.sum(speed[:, 0, :])
    slab_flux = butterfly_sum(jnp.full((8, 128), local_flux, jnp.float32), "space")
    start = (jnp.zeros((3, BINS_DEV), jnp.float32), jnp.zeros((BINS_DEV,), jnp.float32))
    chunks = 4
    steps = tiles // group // chunks
    momentum, counts = start
    for chunk in range(chunks):
        piece = slice(chunk * steps, (chunk + 1) * steps)
        (part_momentum, part_counts), unused = lax.scan(
            accumulate, start, (grouped_speed[piece], grouped_bins[piece])
        )
        momentum = momentum + part_momentum
        counts = counts + part_counts
    packed = jnp.concatenate(
        [momentum, counts[None, :], jnp.full((4, BINS_DEV), slab_flux[0, 0], jnp.float32)], axis=0
    )
    packed = butterfly_sum(packed, "rep")
    momentum, counts = packed[0:3], packed[3]
    flux_sum = packed[4, 0]
    bin_velocity = momentum / counts[None, :]
    total_beads = lax.axis_size("rep") * lax.axis_size("space") * tiles * width
    inflow = 2.0 * TARGET_FLOW - flux_sum / total_beads
    slots = jnp.arange(thermal.shape[-1], dtype=jnp.int32)
    live = slots[None, :] < slot_counts[:, None]
    lift = jnp.where(jnp.arange(3)[:, None] == 0, inflow, jnp.float32(0.0))
    inserted = jnp.where(live[:, None, :], thermal + lift[None], jnp.float32(0.0))
    return (place[None], speed[None], bin_velocity, inserted)


def solution(mesh):
    return jax.shard_map(
        shards,
        mesh=mesh,
        in_specs=(
            P("rep", "space", None, None),
            P("rep", "space", None, None),
            P("rep", "space", None),
            P(None, "rep", "space", None),
            P("rep", "space", None),
            P("rep", "space", None),
            P("rep", None, None),
            P("rep"),
        ),
        out_specs=(
            P("rep", "space", None, None),
            P("rep", "space", None, None),
            P(None, "space"),
            P("rep", None, None),
        ),
        check_vma=False,
    )
```

```python
import jax
import jax.numpy as jnp
from jax import lax
from jax.sharding import PartitionSpec as P

HALO = 16
BINS_DEV = 1024


TIME_STEP = 0.02
REPULSION = 0.25
FRICTION = 1.0
NOISE_AMP = 0.25
SPACING = 0.02
TARGET_FLOW = 1.0


def padded(value, sides, width):
    for axis, dim in sides:
        count, length = (lax.axis_size(axis), value.shape[dim])
        up = [(i, (i + 1) % count) for i in range(count - 1)]
        down = [(j, i) for i, j in up]
        last = lax.slice_in_dim(value, length - width, length, axis=dim)
        initial = lax.slice_in_dim(value, 0, width, axis=dim)
        before = lax.ppermute(last, axis, up)
        after = lax.ppermute(initial, axis, down)
        value = jnp.concatenate([before, value, after], axis=dim)
    return value


def butterfly_sum(value, axis, radix=2):
    count = lax.axis_size(axis)
    stride = 1
    while stride < count:
        group = min(radix, count // stride)
        leaves = [value]
        for j in range(1, group):
            pairs = [(i, i ^ (j * stride)) for i in range(count)]
            leaves.append(lax.ppermute(value, axis, pairs))
        while len(leaves) > 1:
            leaves = [leaves[k] + leaves[k + 1] for k in range(0, len(leaves), 2)]
        value = leaves[0]
        stride *= group
    return value


def bead_forces(own_tile, partners, shift_x):
    offset_x = own_tile[0][None, :, None] - partners[:, 0][:, None, :] + shift_x[:, None, None]
    offset_y = own_tile[1][None, :, None] - partners[:, 1][:, None, :]
    offset_z = own_tile[2][None, :, None] - partners[:, 2][:, None, :]
    closing = offset_x * (own_tile[3][None, :, None] - partners[:, 3][:, None, :])
    closing = closing + offset_y * (own_tile[4][None, :, None] - partners[:, 4][:, None, :])
    closing = closing + offset_z * (own_tile[5][None, :, None] - partners[:, 5][:, None, :])
    weight = jnp.maximum(
        1.0 - (offset_x * offset_x + offset_y * offset_y + offset_z * offset_z), 0.0
    )
    kicks = own_tile[7][None, :, None] + partners[:, 7][:, None, :]
    factor = own_tile[6][None, :, None] * partners[:, 6][:, None, :] * weight
    factor = factor * (REPULSION - FRICTION * weight * closing + NOISE_AMP * kicks)
    return jnp.stack(
        [
            jnp.sum(factor * offset_x, axis=(0, 2)),
            jnp.sum(factor * offset_y, axis=(0, 2)),
            jnp.sum(factor * offset_z, axis=(0, 2)),
        ]
    )


def tile_forces(source, own_tiles, own_index, link_index):
    tiles = own_index.shape[0]
    group = 32
    width = source.shape[-1]

    def per_group(item):
        own_group, link_group, index_group = item
        partners = source[link_group]
        shifts = SPACING * (index_group[:, None] - link_group).astype(jnp.float32)
        return jax.vmap(bead_forces)(own_group, partners, shifts)

    result = lax.map(
        per_group,
        (
            own_tiles.reshape(tiles // group, group, 8, width),
            link_index.reshape(tiles // group, group, link_index.shape[1]),
            own_index.reshape(tiles // group, group),
        ),
    )
    return result.reshape(tiles, 3, width)


def shards(positions, velocities, strength, noise, neighbours, bins, thermal, slot_counts):
    place = positions[0]
    speed = velocities[0]
    weights = strength[0]
    links = neighbours[0]
    substeps = noise.shape[0]
    tiles = links.shape[0]
    count = lax.axis_size("space")
    up = [(i, i + 1) for i in range(count - 1)]
    down = [(i + 1, i) for i in range(count - 1)]
    local = jnp.arange(tiles, dtype=jnp.int32)
    inner = local[HALO : tiles - HALO]
    outer = jnp.concatenate([local[:HALO], local[tiles - HALO :]])
    inner_links = links[HALO : tiles - HALO] - HALO
    outer_links = jnp.concatenate([links[:HALO], links[tiles - HALO :]], axis=0)
    for substep in range(substeps):
        packed = jnp.concatenate(
            [place, speed, weights[:, None, :], noise[substep, 0][:, None, :]], axis=1
        )
        before = lax.ppermute(packed[tiles - HALO :], "space", up)
        after = lax.ppermute(packed[:HALO], "space", down)
        inner_force = tile_forces(packed, packed[HALO : tiles - HALO], inner, inner_links)
        extended = jnp.concatenate([before, packed, after], axis=0)
        outer_tiles = jnp.concatenate([packed[:HALO], packed[tiles - HALO :]], axis=0)
        outer_force = tile_forces(extended, outer_tiles, outer + HALO, outer_links)
        force = jnp.concatenate(
            [outer_force[:HALO], inner_force, outer_force[HALO:]], axis=0
        )
        speed = speed + TIME_STEP * force
        place = place + TIME_STEP * speed
    tiles = speed.shape[0]
    width = speed.shape[-1]
    group = 8
    labels = jnp.arange(BINS_DEV, dtype=jnp.int32)
    grouped_speed = speed.reshape(tiles // group, group, 3, width)
    grouped_bins = bins[0].reshape(tiles // group, group * width)

    def accumulate(carry, item):
        momentum, counts = carry
        block_speed, block_bins = item
        table = (block_bins[:, None] == labels[None, :]).astype(jnp.float32)
        rows_now = jnp.transpose(block_speed, (1, 0, 2)).reshape(3, group * width)
        momentum = momentum + jnp.dot(
            rows_now, table, precision=lax.Precision.HIGHEST, preferred_element_type=jnp.float32
        )
        counts = counts + jnp.sum(table, axis=0)
        return ((momentum, counts), None)

    local_flux = jnp.sum(speed[:, 0, :])
    slab_flux = butterfly_sum(jnp.full((8, 128), local_flux, jnp.float32), "space")
    start = (jnp.zeros((3, BINS_DEV), jnp.float32), jnp.zeros((BINS_DEV,), jnp.float32))
    chunks = 4
    steps = tiles // group // chunks
    momentum, counts = start
    for chunk in range(chunks):
        piece = slice(chunk * steps, (chunk + 1) * steps)
        (part_momentum, part_counts), unused = lax.scan(
            accumulate, start, (grouped_speed[piece], grouped_bins[piece])
        )
        momentum = momentum + part_momentum
        counts = counts + part_counts
    packed = jnp.concatenate(
        [momentum, counts[None, :], jnp.full((4, BINS_DEV), slab_flux[0, 0], jnp.float32)], axis=0
    )
    packed = butterfly_sum(packed, "rep")
    momentum, counts = packed[0:3], packed[3]
    flux_sum = packed[4, 0]
    bin_velocity = momentum / counts[None, :]
    total_beads = lax.axis_size("rep") * lax.axis_size("space") * tiles * width
    inflow = 2.0 * TARGET_FLOW - flux_sum / total_beads
    slots = jnp.arange(thermal.shape[-1], dtype=jnp.int32)
    live = slots[None, :] < slot_counts[:, None]
    lift = jnp.where(jnp.arange(3)[:, None] == 0, inflow, jnp.float32(0.0))
    inserted = jnp.where(live[:, None, :], thermal + lift[None], jnp.float32(0.0))
    return (place[None], speed[None], bin_velocity, inserted)


def solution(mesh):
    return jax.shard_map(
        shards,
        mesh=mesh,
        in_specs=(
            P("rep", "space", None, None),
            P("rep", "space", None, None),
            P("rep", "space", None),
            P(None, "rep", "space", None),
            P("rep", "space", None),
            P("rep", "space", None),
            P("rep", None, None),
            P("rep"),
        ),
        out_specs=(
            P("rep", "space", None, None),
            P("rep", "space", None, None),
            P(None, "space"),
            P("rep", None, None),
        ),
        check_vma=False,
    )
```
